256 devices in a mesh: row: 4 (over x), col: 16 (over y_lo, z), batch: 4 (over y_hi, core).
Axes of the slice: x: 4, y: 4 (y_hi: 2, y_lo: 2; y = y_hi * 2 + y_lo), z: 8, core: 2. Of those that a mesh axis runs over, the one named last changes fastest.
Arguments:
- grid_feats: bfloat16 [4, 128, 1024, 128], P('batch', 'row', 'col'), may hold values from -6 to 6
- station_values: bfloat16 [4, 40960, 512], P('batch', ('row', 'col')), may hold values from -6 to 6
- station_tile: int32 [4, 40960, 1], P('batch', ('row', 'col')), may hold values from 0 to 63; in each aligned block of 640 rows (0 to 639, 640 to 1279, ..., all dimensions but the last counted through in order) at most 20 rows name the same one
- station_cell: int32 [4, 40960], P('batch', ('row', 'col')), may hold values from 0 to 2047
- w_embed: bfloat16 [512, 128], replicated, may hold values from -0.25 to 0.25
- w_first: bfloat16 [3, 3, 128, 128], replicated, may hold values from -0.1875 to 0.1875
- w_second: bfloat16 [3, 3, 128, 128], replicated, may hold values from -0.1875 to 0.1875
- cotangent: bfloat16 [4, 128, 1024, 128], P('batch', 'row', 'col'), may hold values from -6 to 6
Outputs:
- output: bfloat16 [4, 128, 1024, 128], P('batch', 'row', 'col')
- grad_first: float32 [3, 3, 128, 128], replicated
- grad_second: float32 [3, 3, 128, 128], replicated
The draws below stay inside these ranges and needn't reach their ends.
Inputs may be any that keep to these rules, and one draw needn't show every extreme that they name: `station_tile`: within the 640 reports of one device (aligned blocks of 640 rows), at most 20 name the same tile, a bound that some block reaches.
All inputs are finite; a program needn't handle non-finite values.
Results may differ from the reference program's by a relative error of at most 0.0054.
Values may be sent and summed in bfloat16 or wider, within the bound.
No kernel may reach another device: no remote copies, remote signals or barrier semaphores. Data moves between devices by JAX's collectives and lax.ppermute only.
A program may use at most 128 MiB of HBM per device.

```python
import math
import jax
import jax.numpy as jnp
import numpy as np
from jax import lax

C = 128
S = 512
CELL_R = 32
CELL_C = 64
ST_DEV = 640
TILE_COLS = 16
TILES = 64
CAP = 20
STATIONS = 40960
BATCH = 4
NR = 128
NC = 1024


def with_ends(entries, key, smallest, top_value):
    spot = [jax.random.randint(jax.random.fold_in(key, axis), (), 0, length) for axis, length in enumerate(entries.shape)]
    longest = entries.shape.index(max(entries.shape))
    neighbour = spot[:longest] + [(spot[longest] + 1) % entries.shape[longest]] + spot[longest + 1:]
    return entries.at[tuple(spot)].set(smallest).at[tuple(neighbour)].set(top_value)


def steps_of(own_key, extent, pieces, least, top_value):
    factor_of = 1.0
    for axis_at, parts in pieces:
        heights = jax.random.uniform(jax.random.fold_in(jax.random.fold_in(own_key, 6), axis_at), (parts,), jnp.float32, least / len(pieces), top_value / len(pieces))
        factor_of = factor_of * jnp.repeat(jnp.exp(heights), extent[axis_at] // parts).reshape((-1,) + (1,) * (len(extent) - 1 - axis_at))
    return factor_of


def assign_block(own_key, own, number, rows, number_of, top, most, skew):
    ranking = jax.random.permutation(own_key, number_of)
    heavy_load, common = portions_of(number_of, rows * top, most, skew, True), portions_of(number_of, rows * top, most, skew, False)
    places = jnp.arange(number_of)

    def named(sizes, turn):
        used = int((sizes > 0).sum())
        fixed = max(1, used // 4)
        shifted = fixed + (places - fixed + turn * (used - fixed)) % max(1, number_of - fixed)
        return jnp.zeros((number_of,), jnp.int32).at[ranking[jnp.where(places < fixed, places, shifted)]].set(jnp.asarray(sizes, jnp.int32))

    sizes = jnp.where(number % 4 == 0, named(heavy_load, number // 4), named(common, number - number // 4 - 1))
    mixed = jax.random.permutation(jax.random.fold_in(own, 3), number_of)
    giver, sink = mixed[0:number_of // 2 * 2:2], mixed[1:number_of // 2 * 2:2]
    room = jnp.minimum(sizes[giver] - 1, most - sizes[sink]) // 2
    room = jnp.where((giver == ranking[0]) | (sink == ranking[0]) | (sizes[sink] == 0), 0, jnp.maximum(room, 0))
    shifted = jax.random.randint(jax.random.fold_in(own, 4), (number_of // 2,), 0, 1 << 20) % (room + 1)
    sizes = sizes.at[giver].add(-shifted).at[sink].add(shifted)
    members = jnp.searchsorted(jnp.cumsum(sizes), jnp.arange(rows * top), side="right").astype(jnp.int32)
    grid = members.reshape(top, rows).T
    grid = grid[jax.random.permutation(jax.random.fold_in(own, 1), rows)]
    turn = jax.random.randint(jax.random.fold_in(own, 2), (rows, 1), 0, top)
    return jnp.take_along_axis(grid, (jnp.arange(top)[None, :] + turn) % top, axis=1)


def portions_of(number_of, total, limit, lean, full):
    loads = [(1 << 20) // math.isqrt(rank ** lean) + 1 for rank in range(1, number_of + 1)]
    largest = limit if full else min(limit, max(-(-total // number_of), total * loads[0] // sum(loads)))
    least = 1 if total - largest >= number_of - 1 else 0
    given, rest = [largest] + [least] * (number_of - 1), total - largest - least * (number_of - 1)
    while rest > 0:
        candidates = [i for i in range(1, number_of) if given[i] < largest] or [i for i in range(1, number_of) if given[i] < limit]
        whole, remaining = sum([loads[i] for i in candidates]), rest
        for i in candidates:
            more = min(limit - given[i], max(1, remaining * loads[i] // whole), rest)
            given[i] = given[i] + more
            rest = rest - more
    return np.array(given)


def bell_draw(key, extent, deviation, reach, shards=(), kind=jnp.bfloat16):
    values = jax.random.normal(key, extent, jnp.float32) * deviation
    if len(shards) > 0:
        values = steps_of(key, extent, shards, -0.22, 0.18) * values
    return jnp.clip(values, min=-reach, max=reach).astype(kind)


def setup_inputs(seed: int = 0) -> dict:
    key_of = jax.random.split(jax.random.key(seed), 9)
    grid_feats = bell_draw(key_of[0], (BATCH, NR, NC, C), 1.0, 6.0, ((0, 4), (1, 4), (2, 16)))
    station_values = bell_draw(key_of[1], (BATCH, STATIONS, S), 1.0, 6.0, ((0, 4), (1, 64)))
    station_tile_keys = jax.random.split(jax.random.fold_in(key_of[2], 1), BATCH * STATIONS // ST_DEV)
    station_tile_turns = jax.random.permutation(jax.random.fold_in(key_of[2], 3), BATCH * STATIONS // ST_DEV)
    station_tile = jax.vmap(lambda own, number: assign_block(jax.random.fold_in(key_of[2], 2), own, number, ST_DEV, TILES, 1, CAP, 2))(station_tile_keys, station_tile_turns).reshape((BATCH, STATIONS, 1))
    station_cell = with_ends(jax.random.randint(key_of[3], (BATCH, STATIONS), 0, CELL_R * CELL_C), jax.random.fold_in(key_of[3], 1), 0, (CELL_R * CELL_C) - 1).astype(jnp.int32)
    w_embed = bell_draw(key_of[4], (S, C), S ** -0.5, 0.25)
    w_first = bell_draw(key_of[5], (3, 3, C, C), (9 * C) ** -0.5, 0.1875)
    w_second = bell_draw(key_of[6], (3, 3, C, C), (9 * C) ** -0.5, 0.1875)
    cotangent = bell_draw(key_of[7], (BATCH, NR, NC, C), 1.0, 6.0, ((0, 4), (1, 4), (2, 16)))
    return {"grid_feats": grid_feats, "station_values": station_values, "station_tile": station_tile, "station_cell": station_cell, "w_embed": w_embed, "w_first": w_first, "w_second": w_second, "cotangent": cotangent}


def conv(field, kernel, step):
    result = lax.conv_general_dilated(field[None].astype(jnp.float32), kernel.astype(jnp.float32), (1, 1), ((step, step), (step, step)), rhs_dilation=(step, step), dimension_numbers=('NHWC', 'HWIO', 'NHWC'), precision=lax.Precision.HIGHEST)
    return result[0]

def kernel_grad(field, back, step):
    rows, cols = (back.shape[0], back.shape[1])
    padded = jnp.pad(field.astype(jnp.float32), ((step, step), (step, step), (0, 0)))
    back_wide = back.astype(jnp.float32)
    blocks = []
    for u in range(3):
        for q in range(3):
            window = padded[step * u:step * u + rows, step * q:step * q + cols, :]
            blocks.append(jnp.einsum('ijc,ijd->cd', window, back_wide, precision=lax.Precision.HIGHEST))
    return jnp.stack(blocks).reshape(3, 3, back.shape[2], back.shape[2])

def reference(grid_feats, station_values, station_tile, station_cell, w_embed, w_first, w_second, cotangent):
    w_turned = jnp.transpose(w_second[::-1, ::-1], (0, 1, 3, 2))

    def one_sample(carry, sample):
        embedded = jnp.dot(station_values[sample], w_embed, preferred_element_type=jnp.float32)
        tile = station_tile[sample, :, 0]
        cell = station_cell[sample]
        grid_row = tile // TILE_COLS * CELL_R + cell // CELL_C
        grid_col = tile % TILE_COLS * CELL_C + cell % CELL_C
        flat = (grid_row * NC + grid_col).astype(jnp.int32)
        placed = jax.ops.segment_sum(embedded, flat, num_segments=NR * NC)
        first_in = (grid_feats[sample].astype(jnp.float32).reshape(NR * NC, C) + placed).astype(jnp.bfloat16).reshape(NR, NC, C)
        pre1 = conv(first_in, w_first, 1)
        act1 = jax.nn.silu(pre1).astype(jnp.bfloat16)
        pre2 = conv(act1, w_second, 2)
        output = (act1.astype(jnp.float32) + pre2).astype(jnp.bfloat16)
        back = cotangent[sample]
        grad_act1 = back.astype(jnp.float32) + conv(back, w_turned, 2)
        sig = jax.nn.sigmoid(pre1)
        grad_pre1 = (grad_act1 * sig * (1.0 + pre1 * (1.0 - sig))).astype(jnp.bfloat16)
        first_sum = carry[0] + kernel_grad(first_in, grad_pre1, 1)
        second_sum = carry[1] + kernel_grad(act1, back, 2)
        return ((first_sum, second_sum), output)
    zeros = jnp.zeros((3, 3, C, C), jnp.float32)
    sums, outputs = lax.scan(one_sample, (zeros, zeros), jnp.arange(BATCH, dtype=jnp.int32))
    scale = 1.0 / math.sqrt(BATCH * NR * NC)
    return (outputs, sums[0] * scale, sums[1] * scale)
```

```python
import math

import jax
import jax.numpy as jnp
from jax import lax
from jax.sharding import PartitionSpec as P


def with_halo(array, sides, width):
    for axis, dim in sides:
        count, length = (lax.axis_size(axis), array.shape[dim])
        up = [(i, (i + 1) % count) for i in range(count - 1)]
        down = [(j, i) for i, j in up]
        last = lax.slice_in_dim(array, length - width, length, axis=dim)
        leading = lax.slice_in_dim(array, 0, width, axis=dim)
        before = lax.ppermute(last, axis, up)
        after = lax.ppermute(leading, axis, down)
        array = jnp.concatenate([before, array, after], axis=dim)
    return array


def halving_steps():
    steps = [("batch", 1)]
    for axis in ("row", "col"):
        d = 1
        while d < lax.axis_size(axis):
            steps.append((axis, d))
            d *= 2
    d = 2
    while d < lax.axis_size("batch"):
        steps.append(("batch", d))
        d *= 2
    return steps


def tree_sum(x):
    steps = halving_steps()
    for axis, d in steps:
        pairs = [(i, i ^ d) for i in range(lax.axis_size(axis))]
        upper = (lax.axis_index(axis) // d) % 2 == 1
        half = x.shape[0] // 2
        low, high = x[:half], x[half:]
        kept = jnp.where(upper, high, low)
        sent = jnp.where(upper, low, high)
        x = kept + lax.ppermute(sent, axis, pairs)
    for axis, d in steps[::-1]:
        pairs = [(i, i ^ d) for i in range(lax.axis_size(axis))]
        upper = (lax.axis_index(axis) // d) % 2 == 1
        got = lax.ppermute(x, axis, pairs)
        x = jnp.where(upper, jnp.concatenate([got, x]), jnp.concatenate([x, got]))
    return x


def unfold(padded, step, rows, cols):
    windows = [
        padded[step * u : step * u + rows, step * q : step * q + cols, :]
        for u in range(3)
        for q in range(3)
    ]
    return jnp.concatenate(windows, axis=-1).reshape(rows * cols, -1)


def contract_rows(left, right):
    return lax.dot_general(
        left, right, (((0,), (0,)), ((), ())), preferred_element_type=jnp.float32
    )


def on_device(
    grid_feats, station_values, station_tile, station_cell, w_embed, w_first, w_second, cotangent
):
    cells = grid_feats[0]
    rows, cols, chans = cells.shape
    values = station_values[0]
    tiles = station_tile[0, :, 0]
    where = station_cell[0]
    n_tiles = lax.axis_size("row") * lax.axis_size("col")
    count = values.shape[0]
    capacity = max(2, 2 * count // n_tiles)
    slots = n_tiles * capacity
    hits = (tiles[:, None] == jnp.arange(n_tiles, dtype=jnp.int32)[None, :]).astype(jnp.int32)
    ranks = jnp.sum(jnp.cumsum(hits, axis=0) * hits, axis=1) - 1
    target = tiles * capacity + ranks
    cell_ids = jnp.zeros((slots,), jnp.int32).at[target].set(where)
    local_rows = jnp.dot(values, w_embed, preferred_element_type=jnp.float32)
    outgoing = jnp.zeros((slots, chans), jnp.float32).at[target].set(local_rows)
    embedded, arrived_ids = (
        lax.all_to_all(outgoing, ("row", "col"), split_axis=0, concat_axis=0, tiled=True),
        lax.all_to_all(cell_ids, ("row", "col"), split_axis=0, concat_axis=0, tiled=True),
    )
    placed = jax.ops.segment_sum(embedded, arrived_ids, num_segments=rows * cols)
    first_in = (
        (cells.astype(jnp.float32).reshape(rows * cols, chans) + placed)
        .astype(jnp.bfloat16)
        .reshape(rows, cols, chans)
    )
    w_one = w_first.reshape(9 * chans, chans)
    w_two = w_second.reshape(9 * chans, chans)
    deep = with_halo(first_in, (("row", 0), ("col", 1)), 3)
    pre_wide = jnp.dot(
        unfold(deep, 1, rows + 4, cols + 4), w_one, preferred_element_type=jnp.float32
    ).reshape(rows + 4, cols + 4, chans)
    row_ids = lax.axis_index("row") * rows - 2 + jnp.arange(rows + 4, dtype=jnp.int32)
    col_ids = lax.axis_index("col") * cols - 2 + jnp.arange(cols + 4, dtype=jnp.int32)
    inside_rows = (row_ids >= 0) & (row_ids < rows * lax.axis_size("row"))
    inside_cols = (col_ids >= 0) & (col_ids < cols * lax.axis_size("col"))
    inside = inside_rows[:, None] & inside_cols[None, :]
    padded1 = jnp.where(inside[:, :, None], jax.nn.silu(pre_wide), 0.0).astype(jnp.bfloat16)
    pre1 = pre_wide[2:-2, 2:-2].reshape(rows * cols, chans)
    act1 = padded1[2:-2, 2:-2]
    patches0 = unfold(deep[2:-2, 2:-2], 1, rows, cols)
    patches1 = unfold(padded1, 2, rows, cols)
    pre2 = jnp.dot(patches1, w_two, preferred_element_type=jnp.float32)
    output = (
        (act1.astype(jnp.float32).reshape(rows * cols, chans) + pre2)
        .astype(jnp.bfloat16)
        .reshape(1, rows, cols, chans)
    )
    back = cotangent[0]
    padded_back = with_halo(back, (("row", 0), ("col", 1)), 2)
    w_turned = jnp.transpose(w_second[::-1, ::-1], (0, 1, 3, 2)).reshape(9 * chans, chans)
    back_flat = back.reshape(rows * cols, chans)
    grad_act1 = back_flat.astype(jnp.float32) + jnp.dot(
        unfold(padded_back, 2, rows, cols), w_turned, preferred_element_type=jnp.float32
    )
    sigmoid_pre = jax.nn.sigmoid(pre1)
    grad_pre1 = (grad_act1 * sigmoid_pre * (1.0 + pre1 * (1.0 - sigmoid_pre))).astype(jnp.bfloat16)
    first_term = contract_rows(patches0, grad_pre1)
    second_term = contract_rows(patches1, back_flat)
    first_sum, second_sum = jnp.split(tree_sum(jnp.concatenate([first_term, second_term])), 2)
    total_cells = (
        rows
        * lax.axis_size("row")
        * cols
        * lax.axis_size("col")
        * lax.axis_size("batch")
        * cells_per_sample_factor(grid_feats)
    )
    scale = 1.0 / math.sqrt(total_cells)
    grad_first = (first_sum * scale).reshape(3, 3, chans, chans)
    grad_second = (second_sum * scale).reshape(3, 3, chans, chans)
    return (output, grad_first, grad_second)


def cells_per_sample_factor(grid_feats):
    return grid_feats.shape[0]


def solution(mesh):
    return jax.shard_map(
        on_device,
        mesh=mesh,
        in_specs=(
            P("batch", "row", "col", None),
            P("batch", ("row", "col"), None),
            P("batch", ("row", "col"), None),
            P("batch", ("row", "col")),
            P(),
            P(),
            P(),
            P("batch", "row", "col", None),
        ),
        out_specs=(P("batch", "row", "col", None), P(), P()),
        check_vma=False,
    )
```

```python
import math

import jax
import jax.numpy as jnp
from jax import lax
from jax.sharding import PartitionSpec as P


def with_halo(array, sides, width):
    for axis, dim in sides:
        count, length = (lax.axis_size(axis), array.shape[dim])
        up = [(i, (i + 1) % count) for i in range(count - 1)]
        down = [(j, i) for i, j in up]
        last = lax.slice_in_dim(array, length - width, length, axis=dim)
        leading = lax.slice_in_dim(array, 0, width, axis=dim)
        before = lax.ppermute(last, axis, up)
        after = lax.ppermute(leading, axis, down)
        array = jnp.concatenate([before, array, after], axis=dim)
    return array


def halving_steps():
    steps = [("batch", 1)]
    for axis in ("row", "col"):
        d = 1
        while d < lax.axis_size(axis):
            steps.append((axis, d))
            d *= 2
    d = 2
    while d < lax.axis_size("batch"):
        steps.append(("batch", d))
        d *= 2
    return steps


def tree_sum(x):
    steps = halving_steps()
    for axis, d in steps:
        pairs = [(i, i ^ d) for i in range(lax.axis_size(axis))]
        upper = (lax.axis_index(axis) // d) % 2 == 1
        half = x.shape[0] // 2
        side = upper.astype(jnp.int32)
        kept = lax.dynamic_slice_in_dim(x, side * half, half)
        sent = lax.dynamic_slice_in_dim(x, (1 - side) * half, half)
        x = kept + lax.ppermute(sent, axis, pairs)
    for axis, d in steps[::-1]:
        pairs = [(i, i ^ d) for i in range(lax.axis_size(axis))]
        upper = (lax.axis_index(axis) // d) % 2 == 1
        got = lax.ppermute(x, axis, pairs)
        both = jnp.stack([x, got])
        side = upper.astype(jnp.int32)
        x = jnp.concatenate(
            [lax.dynamic_index_in_dim(both, side, keepdims=False),
             lax.dynamic_index_in_dim(both, 1 - side, keepdims=False)]
        )
    return x


def unfold(padded, step, rows, cols):
    windows = [
        padded[step * u : step * u + rows, step * q : step * q + cols, :]
        for u in range(3)
        for q in range(3)
    ]
    return jnp.concatenate(windows, axis=-1).reshape(rows * cols, -1)


def contract_rows(left, right):
    return lax.dot_general(
        left, right, (((0,), (0,)), ((), ())), preferred_element_type=jnp.float32
    )


def on_device(
    grid_feats, station_values, station_tile, station_cell, w_embed, w_first, w_second, cotangent
):
    cells = grid_feats[0]
    rows, cols, chans = cells.shape
    values = station_values[0]
    tiles = station_tile[0, :, 0]
    where = station_cell[0]
    n_tiles = lax.axis_size("row") * lax.axis_size("col")
    count = values.shape[0]
    capacity = max(2, 2 * count // n_tiles)
    slots = n_tiles * capacity
    hits = (tiles[:, None] == jnp.arange(n_tiles, dtype=jnp.int32)[None, :]).astype(jnp.int32)
    ranks = jnp.sum(jnp.cumsum(hits, axis=0) * hits, axis=1) - 1
    target = tiles * capacity + ranks
    chooser = (target[None, :] == jnp.arange(slots, dtype=jnp.int32)[:, None]).astype(jnp.bfloat16)
    chosen = jnp.dot(chooser, values, preferred_element_type=jnp.float32).astype(jnp.bfloat16)
    outgoing = jnp.dot(chosen, w_embed, preferred_element_type=jnp.float32)
    id_parts = jnp.zeros((count, chans), jnp.bfloat16)
    id_parts = id_parts.at[:, 0].set((where // 64 * 64).astype(jnp.bfloat16))
    id_parts = id_parts.at[:, 1].set((where % 64).astype(jnp.bfloat16))
    id_sums = jnp.dot(chooser, id_parts, preferred_element_type=jnp.float32)
    slot_ids = (id_sums[:, 0] + id_sums[:, 1]).reshape(n_tiles, capacity)
    id_row = jnp.zeros((n_tiles, 1, chans), jnp.float32).at[:, 0, :capacity].set(slot_ids)
    payload = jnp.concatenate([outgoing.reshape(n_tiles, capacity, chans), id_row], axis=1)
    arrived = lax.all_to_all(payload, ("row", "col"), split_axis=0, concat_axis=0, tiled=True)
    embedded = arrived[:, :capacity, :].reshape(slots, chans)
    arrived_ids = arrived[:, capacity, :capacity].reshape(slots)
    spread = (
        arrived_ids[None, :] == jnp.arange(rows * cols, dtype=jnp.float32)[:, None]
    ).astype(jnp.bfloat16)
    top = embedded.astype(jnp.bfloat16)
    rest = embedded - top.astype(jnp.float32)
    middle = rest.astype(jnp.bfloat16)
    bottom = (rest - middle.astype(jnp.float32)).astype(jnp.bfloat16)
    pieces = jnp.dot(
        spread, jnp.concatenate([top, middle, bottom], axis=1), preferred_element_type=jnp.float32
    )
    placed = pieces[:, :chans] + pieces[:, chans : 2 * chans] + pieces[:, 2 * chans :]
    first_in = (
        (cells.astype(jnp.float32).reshape(rows * cols, chans) + placed)
        .astype(jnp.bfloat16)
        .reshape(rows, cols, chans)
    )
    w_one = w_first.reshape(9 * chans, chans)
    w_two = w_second.reshape(9 * chans, chans)
    deep = with_halo(first_in, (("row", 0), ("col", 1)), 3)
    pre_wide = jnp.dot(
        unfold(deep, 1, rows + 4, cols + 4), w_one, preferred_element_type=jnp.float32
    ).reshape(rows + 4, cols + 4, chans)
    row_ids = lax.axis_index("row") * rows - 2 + jnp.arange(rows + 4, dtype=jnp.int32)
    col_ids = lax.axis_index("col") * cols - 2 + jnp.arange(cols + 4, dtype=jnp.int32)
    inside_rows = (row_ids >= 0) & (row_ids < rows * lax.axis_size("row"))
    inside_cols = (col_ids >= 0) & (col_ids < cols * lax.axis_size("col"))
    inside = inside_rows[:, None] & inside_cols[None, :]
    padded1 = jnp.where(inside[:, :, None], jax.nn.silu(pre_wide), 0.0).astype(jnp.bfloat16)
    pre1 = pre_wide[2:-2, 2:-2].reshape(rows * cols, chans)
    act1 = padded1[2:-2, 2:-2]
    patches0 = unfold(deep[2:-2, 2:-2], 1, rows, cols)
    patches1 = unfold(padded1, 2, rows, cols)
    pre2 = jnp.dot(patches1, w_two, preferred_element_type=jnp.float32)
    output = (
        (act1.astype(jnp.float32).reshape(rows * cols, chans) + pre2)
        .astype(jnp.bfloat16)
        .reshape(1, rows, cols, chans)
    )
    back = cotangent[0]
    padded_back = with_halo(back, (("row", 0), ("col", 1)), 2)
    w_turned = jnp.transpose(w_second[::-1, ::-1], (0, 1, 3, 2)).reshape(9 * chans, chans)
    back_flat = back.reshape(rows * cols, chans)
    grad_act1 = back_flat.astype(jnp.float32) + jnp.dot(
        unfold(padded_back, 2, rows, cols), w_turned, preferred_element_type=jnp.float32
    )
    sigmoid_pre = jax.nn.sigmoid(pre1)
    grad_pre1 = (grad_act1 * sigmoid_pre * (1.0 + pre1 * (1.0 - sigmoid_pre))).astype(jnp.bfloat16)
    first_term = contract_rows(patches0, grad_pre1)
    second_term = contract_rows(patches1, back_flat)
    first_sum, second_sum = jnp.split(tree_sum(jnp.concatenate([first_term, second_term])), 2)
    total_cells = (
        rows
        * lax.axis_size("row")
        * cols
        * lax.axis_size("col")
        * lax.axis_size("batch")
        * cells_per_sample_factor(grid_feats)
    )
    scale = 1.0 / math.sqrt(total_cells)
    grad_first = (first_sum * scale).reshape(3, 3, chans, chans)
    grad_second = (second_sum * scale).reshape(3, 3, chans, chans)
    return (output, grad_first, grad_second)


def cells_per_sample_factor(grid_feats):
    return grid_feats.shape[0]


def solution(mesh):
    return jax.shard_map(
        on_device,
        mesh=mesh,
        in_specs=(
            P("batch", "row", "col", None),
            P("batch", ("row", "col"), None),
            P("batch", ("row", "col"), None),
            P("batch", ("row", "col")),
            P(),
            P(),
            P(),
            P("batch", "row", "col", None),
        ),
        out_specs=(P("batch", "row", "col", None), P(), P()),
        check_vma=False,
    )
```

```python
import math

import jax
import jax.numpy as jnp
from jax import lax
from jax.sharding import PartitionSpec as P


def with_halo(array, sides, width):
    for axis, dim in sides:
        count, length = (lax.axis_size(axis), array.shape[dim])
        up = [(i, (i + 1) % count) for i in range(count - 1)]
        down = [(j, i) for i, j in up]
        last = lax.slice_in_dim(array, length - width, length, axis=dim)
        leading = lax.slice_in_dim(array, 0, width, axis=dim)
        before = lax.ppermute(last, axis, up)
        after = lax.ppermute(leading, axis, down)
        array = jnp.concatenate([before, array, after], axis=dim)
    return array


def halving_steps():
    steps = [("batch", 1)]
    for axis in ("row", "col"):
        d = 1
        while d < lax.axis_size(axis):
            steps.append((axis, d))
            d *= 2
    d = 2
    while d < lax.axis_size("batch"):
        steps.append(("batch", d))
        d *= 2
    return steps


def tree_sum(x):
    steps = halving_steps()
    for axis, d in steps:
        pairs = [(i, i ^ d) for i in range(lax.axis_size(axis))]
        upper = (lax.axis_index(axis) // d) % 2 == 1
        half = x.shape[0] // 2
        side = upper.astype(jnp.int32)
        kept = lax.dynamic_slice_in_dim(x, side * half, half)
        sent = lax.dynamic_slice_in_dim(x, (1 - side) * half, half)
        x = kept + lax.ppermute(sent, axis, pairs)
    for axis, d in steps[::-1]:
        pairs = [(i, i ^ d) for i in range(lax.axis_size(axis))]
        upper = (lax.axis_index(axis) // d) % 2 == 1
        got = lax.ppermute(x, axis, pairs)
        both = jnp.stack([x, got])
        side = upper.astype(jnp.int32)
        x = jnp.concatenate(
            [lax.dynamic_index_in_dim(both, side, keepdims=False),
             lax.dynamic_index_in_dim(both, 1 - side, keepdims=False)]
        )
    return x


def unfold(padded, step, rows, cols):
    windows = [
        padded[step * u : step * u + rows, step * q : step * q + cols, :]
        for u in range(3)
        for q in range(3)
    ]
    return jnp.concatenate(windows, axis=-1).reshape(rows * cols, -1)


def contract_rows(left, right):
    return lax.dot_general(
        left, right, (((0,), (0,)), ((), ())), preferred_element_type=jnp.float32
    )


def on_device(
    grid_feats, station_values, station_tile, station_cell, w_embed, w_first, w_second, cotangent
):
    cells = grid_feats[0]
    rows, cols, chans = cells.shape
    values = station_values[0]
    tiles = station_tile[0, :, 0]
    where = station_cell[0]
    n_tiles = lax.axis_size("row") * lax.axis_size("col")
    count = values.shape[0]
    capacity = max(2, 2 * count // n_tiles)
    slots = n_tiles * capacity
    hits = (tiles[:, None] == jnp.arange(n_tiles, dtype=jnp.int32)[None, :]).astype(jnp.int32)
    ranks = jnp.sum(jnp.cumsum(hits, axis=0) * hits, axis=1) - 1
    target = tiles * capacity + ranks
    chooser = (target[None, :] == jnp.arange(slots, dtype=jnp.int32)[:, None]).astype(jnp.bfloat16)
    chosen = jnp.dot(chooser, values, preferred_element_type=jnp.float32).astype(jnp.bfloat16)
    outgoing = jnp.dot(chosen, w_embed, preferred_element_type=jnp.float32)
    id_parts = jnp.zeros((count, chans), jnp.bfloat16)
    id_parts = id_parts.at[:, 0].set((where // 64 * 64).astype(jnp.bfloat16))
    id_parts = id_parts.at[:, 1].set((where % 64).astype(jnp.bfloat16))
    id_sums = jnp.dot(chooser, id_parts, preferred_element_type=jnp.float32)
    slot_ids = (id_sums[:, 0] + id_sums[:, 1]).reshape(n_tiles, capacity)
    id_row = jnp.zeros((n_tiles, 1, chans), jnp.float32).at[:, 0, :capacity].set(slot_ids)
    payload = jnp.concatenate([outgoing.reshape(n_tiles, capacity, chans), id_row], axis=1)
    arrived = lax.all_to_all(payload, ("row", "col"), split_axis=0, concat_axis=0, tiled=True)
    embedded = arrived[:, :capacity, :].reshape(slots, chans)
    arrived_ids = arrived[:, capacity, :capacity].reshape(slots)
    spread = (
        arrived_ids[None, :] == jnp.arange(rows * cols, dtype=jnp.float32)[:, None]
    ).astype(jnp.bfloat16)
    top = lax.reduce_precision(embedded, exponent_bits=8, mantissa_bits=7)
    rest = embedded - top
    middle = lax.reduce_precision(rest, exponent_bits=8, mantissa_bits=7)
    bottom = rest - middle
    split = jnp.concatenate([top, middle, bottom], axis=1).astype(jnp.bfloat16)
    pieces = jnp.dot(spread, split, preferred_element_type=jnp.float32)
    placed = pieces[:, :chans] + pieces[:, chans : 2 * chans] + pieces[:, 2 * chans :]
    first_in = (
        (cells.astype(jnp.float32).reshape(rows * cols, chans) + placed)
        .astype(jnp.bfloat16)
        .reshape(rows, cols, chans)
    )
    w_one = w_first.reshape(9 * chans, chans)
    w_two = w_second.reshape(9 * chans, chans)
    deep = with_halo(first_in, (("row", 0), ("col", 1)), 3)
    pre_wide = jnp.dot(
        unfold(deep, 1, rows + 4, cols + 4), w_one, preferred_element_type=jnp.float32
    ).reshape(rows + 4, cols + 4, chans)
    row_ids = lax.axis_index("row") * rows - 2 + jnp.arange(rows + 4, dtype=jnp.int32)
    col_ids = lax.axis_index("col") * cols - 2 + jnp.arange(cols + 4, dtype=jnp.int32)
    inside_rows = (row_ids >= 0) & (row_ids < rows * lax.axis_size("row"))
    inside_cols = (col_ids >= 0) & (col_ids < cols * lax.axis_size("col"))
    inside = inside_rows[:, None] & inside_cols[None, :]
    padded1 = jnp.where(inside[:, :, None], jax.nn.silu(pre_wide), 0.0).astype(jnp.bfloat16)
    pre1 = pre_wide[2:-2, 2:-2].reshape(rows * cols, chans)
    act1 = padded1[2:-2, 2:-2]
    patches0 = unfold(deep[2:-2, 2:-2], 1, rows, cols)
    patches1 = unfold(padded1, 2, rows, cols)
    pre2 = jnp.dot(patches1, w_two, preferred_element_type=jnp.float32)
    output = (
        (act1.astype(jnp.float32).reshape(rows * cols, chans) + pre2)
        .astype(jnp.bfloat16)
        .reshape(1, rows, cols, chans)
    )
    back = cotangent[0]
    padded_back = with_halo(back, (("row", 0), ("col", 1)), 2)
    w_turned = jnp.transpose(w_second[::-1, ::-1], (0, 1, 3, 2)).reshape(9 * chans, chans)
    back_flat = back.reshape(rows * cols, chans)
    grad_act1 = back_flat.astype(jnp.float32) + jnp.dot(
        unfold(padded_back, 2, rows, cols), w_turned, preferred_element_type=jnp.float32
    )
    sigmoid_pre = jax.nn.sigmoid(pre1)
    grad_pre1 = (grad_act1 * sigmoid_pre * (1.0 + pre1 * (1.0 - sigmoid_pre))).astype(jnp.bfloat16)
    first_term = contract_rows(patches0, grad_pre1)
    second_term = contract_rows(patches1, back_flat)
    first_sum, second_sum = jnp.split(tree_sum(jnp.concatenate([first_term, second_term])), 2)
    total_cells = (
        rows
        * lax.axis_size("row")
        * cols
        * lax.axis_size("col")
        * lax.axis_size("batch")
        * cells_per_sample_factor(grid_feats)
    )
    scale = 1.0 / math.sqrt(total_cells)
    grad_first = (first_sum * scale).reshape(3, 3, chans, chans)
    grad_second = (second_sum * scale).reshape(3, 3, chans, chans)
    return (output, grad_first, grad_second)


def cells_per_sample_factor(grid_feats):
    return grid_feats.shape[0]


def solution(mesh):
    return jax.shard_map(
        on_device,
        mesh=mesh,
        in_specs=(
            P("batch", "row", "col", None),
            P("batch", ("row", "col"), None),
            P("batch", ("row", "col"), None),
            P("batch", ("row", "col")),
            P(),
            P(),
            P(),
            P("batch", "row", "col", None),
        ),
        out_specs=(P("batch", "row", "col", None), P(), P()),
        check_vma=False,
    )
```

```python
import math

import jax
import jax.numpy as jnp
from jax import lax
from jax.sharding import PartitionSpec as P


def with_halo(array, sides, width):
    for axis, dim in sides:
        count, length = (lax.axis_size(axis), array.shape[dim])
        up = [(i, (i + 1) % count) for i in range(count - 1)]
        down = [(j, i) for i, j in up]
        last = lax.slice_in_dim(array, length - width, length, axis=dim)
        leading = lax.slice_in_dim(array, 0, width, axis=dim)
        before = lax.ppermute(last, axis, up)
        after = lax.ppermute(leading, axis, down)
        array = jnp.concatenate([before, array, after], axis=dim)
    return array


def halving_steps():
    steps = [("batch", 1)]
    for axis in ("row", "col"):
        d = 1
        while d < lax.axis_size(axis):
            steps.append((axis, d))
            d *= 2
    d = 2
    while d < lax.axis_size("batch"):
        steps.append(("batch", d))
        d *= 2
    return steps


def tree_sum(x):
    steps = halving_steps()
    for axis, d in steps:
        pairs = [(i, i ^ d) for i in range(lax.axis_size(axis))]
        upper = (lax.axis_index(axis) // d) % 2 == 1
        half = x.shape[0] // 2
        side = upper.astype(jnp.int32)
        kept = lax.dynamic_slice_in_dim(x, side * half, half)
        sent = lax.dynamic_slice_in_dim(x, (1 - side) * half, half)
        x = kept + lax.ppermute(sent, axis, pairs)
    for axis, d in steps[::-1]:
        pairs = [(i, i ^ d) for i in range(lax.axis_size(axis))]
        upper = (lax.axis_index(axis) // d) % 2 == 1
        got = lax.ppermute(x, axis, pairs)
        both = jnp.stack([x, got])
        side = upper.astype(jnp.int32)
        x = jnp.concatenate(
            [lax.dynamic_index_in_dim(both, side, keepdims=False),
             lax.dynamic_index_in_dim(both, 1 - side, keepdims=False)]
        )
    return x


def unfold(padded, step, rows, cols):
    windows = [
        padded[step * u : step * u + rows, step * q : step * q + cols, :]
        for u in range(3)
        for q in range(3)
    ]
    return jnp.concatenate(windows, axis=-1).reshape(rows * cols, -1)


def contract_rows(left, right):
    return lax.dot_general(
        left, right, (((0,), (0,)), ((), ())), preferred_element_type=jnp.float32
    )


def on_device(
    grid_feats, station_values, station_tile, station_cell, w_embed, w_first, w_second, cotangent
):
    cells = grid_feats[0]
    rows, cols, chans = cells.shape
    values = station_values[0]
    tiles = station_tile[0, :, 0]
    where = station_cell[0]
    n_tiles = lax.axis_size("row") * lax.axis_size("col")
    count = values.shape[0]
    capacity = max(2, 2 * count // n_tiles)
    slots = n_tiles * capacity
    hits = (tiles[:, None] == jnp.arange(n_tiles, dtype=jnp.int32)[None, :]).astype(jnp.int32)
    ranks = jnp.sum(jnp.cumsum(hits, axis=0) * hits, axis=1) - 1
    target = tiles * capacity + ranks
    chooser = (target[None, :] == jnp.arange(slots, dtype=jnp.int32)[:, None]).astype(jnp.bfloat16)
    chosen = jnp.dot(chooser, values, preferred_element_type=jnp.float32).astype(jnp.bfloat16)
    outgoing = jnp.dot(chosen, w_embed, preferred_element_type=jnp.float32)
    id_parts = jnp.zeros((count, chans), jnp.bfloat16)
    id_parts = id_parts.at[:, 0].set((where // 64 * 64).astype(jnp.bfloat16))
    id_parts = id_parts.at[:, 1].set((where % 64).astype(jnp.bfloat16))
    id_sums = jnp.dot(chooser, id_parts, preferred_element_type=jnp.float32)
    slot_ids = (id_sums[:, 0] + id_sums[:, 1]).reshape(n_tiles, capacity)
    id_row = jnp.zeros((n_tiles, 1, chans), jnp.float32).at[:, 0, :capacity].set(slot_ids)
    payload = jnp.concatenate([outgoing.reshape(n_tiles, capacity, chans), id_row], axis=1)
    arrived = lax.all_to_all(payload, ("row", "col"), split_axis=0, concat_axis=0, tiled=True)
    embedded = arrived[:, :capacity, :].reshape(slots, chans)
    arrived_ids = arrived[:, capacity, :capacity].reshape(slots)
    spread = (
        arrived_ids[None, :] == jnp.arange(rows * cols, dtype=jnp.float32)[:, None]
    ).astype(jnp.bfloat16)
    top = lax.reduce_precision(embedded, exponent_bits=8, mantissa_bits=7)
    rest = embedded - top
    middle = lax.reduce_precision(rest, exponent_bits=8, mantissa_bits=7)
    bottom = rest - middle
    split = jnp.concatenate([top, middle, bottom], axis=1).astype(jnp.bfloat16)
    pieces = jnp.dot(spread, split, preferred_element_type=jnp.float32)
    placed = pieces[:, :chans] + pieces[:, chans : 2 * chans] + pieces[:, 2 * chans :]
    first_in = (
        (cells.astype(jnp.float32).reshape(rows * cols, chans) + placed)
        .astype(jnp.bfloat16)
        .reshape(rows, cols, chans)
    )
    w_one = w_first.reshape(9 * chans, chans)
    w_two = w_second.reshape(9 * chans, chans)
    deep = with_halo(first_in, (("row", 0), ("col", 1)), 3)
    pre_wide = jnp.dot(
        unfold(deep, 1, rows + 4, cols + 4), w_one, preferred_element_type=jnp.float32
    ).reshape(rows + 4, cols + 4, chans)
    row_ids = lax.axis_index("row") * rows - 2 + jnp.arange(rows + 4, dtype=jnp.int32)
    col_ids = lax.axis_index("col") * cols - 2 + jnp.arange(cols + 4, dtype=jnp.int32)
    inside_rows = (row_ids >= 0) & (row_ids < rows * lax.axis_size("row"))
    inside_cols = (col_ids >= 0) & (col_ids < cols * lax.axis_size("col"))
    inside = inside_rows[:, None] & inside_cols[None, :]
    padded1 = jnp.where(inside[:, :, None], jax.nn.silu(pre_wide), 0.0).astype(jnp.bfloat16)
    pre1 = pre_wide[2:-2, 2:-2].reshape(rows * cols, chans)
    act1 = padded1[2:-2, 2:-2]
    patches0 = unfold(deep[2:-2, 2:-2], 1, rows, cols)
    patches1 = unfold(padded1, 2, rows, cols)
    pre2 = jnp.dot(patches1, w_two, preferred_element_type=jnp.float32)
    output = (
        (act1.astype(jnp.float32).reshape(rows * cols, chans) + pre2)
        .astype(jnp.bfloat16)
        .reshape(1, rows, cols, chans)
    )
    back = cotangent[0]
    padded_back = with_halo(back, (("row", 0), ("col", 1)), 2)
    w_turned = jnp.transpose(w_second[::-1, ::-1], (0, 1, 3, 2)).reshape(9 * chans, chans)
    back_flat = back.reshape(rows * cols, chans)
    grad_act1 = back_flat.astype(jnp.float32) + jnp.dot(
        unfold(padded_back, 2, rows, cols), w_turned, preferred_element_type=jnp.float32
    )
    sigmoid_pre = jax.nn.sigmoid(pre1)
    grad_pre1 = (grad_act1 * sigmoid_pre * (1.0 + pre1 * (1.0 - sigmoid_pre))).astype(jnp.bfloat16)
    grad_pre1 = lax.optimization_barrier(grad_pre1)
    first_term = contract_rows(patches0, grad_pre1)
    second_term = contract_rows(patches1, back_flat)
    first_sum, second_sum = jnp.split(tree_sum(jnp.concatenate([first_term, second_term])), 2)
    total_cells = (
        rows
        * lax.axis_size("row")
        * cols
        * lax.axis_size("col")
        * lax.axis_size("batch")
        * cells_per_sample_factor(grid_feats)
    )
    scale = 1.0 / math.sqrt(total_cells)
    grad_first = (first_sum * scale).reshape(3, 3, chans, chans)
    grad_second = (second_sum * scale).reshape(3, 3, chans, chans)
    return (output, grad_first, grad_second)


def cells_per_sample_factor(grid_feats):
    return grid_feats.shape[0]


def solution(mesh):
    return jax.shard_map(
        on_device,
        mesh=mesh,
        in_specs=(
            P("batch", "row", "col", None),
            P("batch", ("row", "col"), None),
            P("batch", ("row", "col"), None),
            P("batch", ("row", "col")),
            P(),
            P(),
            P(),
            P("batch", "row", "col", None),
        ),
        out_specs=(P("batch", "row", "col", None), P(), P()),
        check_vma=False,
    )
```

```python
import math

import jax
import jax.numpy as jnp
from jax import lax
from jax.sharding import PartitionSpec as P


def with_halo(array, width):
    n_row, n_col = lax.axis_size("row"), lax.axis_size("col")

    def moved(block, d_row, d_col):
        if d_col == 0:
            count = n_row
            pairs = [(i, i + d_row) for i in range(count) if 0 <= i + d_row < count]
            return lax.ppermute(block, "row", pairs)
        if d_row == 0:
            count = n_col
            pairs = [(i, i + d_col) for i in range(count) if 0 <= i + d_col < count]
            return lax.ppermute(block, "col", pairs)
        pairs = [
            (r * n_col + c, (r + d_row) * n_col + c + d_col)
            for r in range(n_row)
            for c in range(n_col)
            if 0 <= r + d_row < n_row and 0 <= c + d_col < n_col
        ]
        return lax.ppermute(block, ("row", "col"), pairs)

    w = width
    north = moved(array[-w:, :], 1, 0)
    south = moved(array[:w, :], -1, 0)
    west = moved(array[:, -w:], 0, 1)
    east = moved(array[:, :w], 0, -1)
    north_west = moved(array[-w:, -w:], 1, 1)
    north_east = moved(array[-w:, :w], 1, -1)
    south_west = moved(array[:w, -w:], -1, 1)
    south_east = moved(array[:w, :w], -1, -1)
    top = jnp.concatenate([north_west, north, north_east], axis=1)
    middle = jnp.concatenate([west, array, east], axis=1)
    bottom = jnp.concatenate([south_west, south, south_east], axis=1)
    return jnp.concatenate([top, middle, bottom], axis=0)


def halving_steps():
    steps = [("batch", 1)]
    for axis in ("row", "col"):
        d = 1
        while d < lax.axis_size(axis):
            steps.append((axis, d))
            d *= 2
    d = 2
    while d < lax.axis_size("batch"):
        steps.append(("batch", d))
        d *= 2
    return steps


def tree_sum(x):
    steps = halving_steps()
    for axis, d in steps:
        pairs = [(i, i ^ d) for i in range(lax.axis_size(axis))]
        upper = (lax.axis_index(axis) // d) % 2 == 1
        half = x.shape[0] // 2
        side = upper.astype(jnp.int32)
        kept = lax.dynamic_slice_in_dim(x, side * half, half)
        sent = lax.dynamic_slice_in_dim(x, (1 - side) * half, half)
        x = kept + lax.ppermute(sent, axis, pairs)
    for axis, d in steps[::-1]:
        pairs = [(i, i ^ d) for i in range(lax.axis_size(axis))]
        upper = (lax.axis_index(axis) // d) % 2 == 1
        got = lax.ppermute(x, axis, pairs)
        both = jnp.stack([x, got])
        side = upper.astype(jnp.int32)
        x = jnp.concatenate(
            [lax.dynamic_index_in_dim(both, side, keepdims=False),
             lax.dynamic_index_in_dim(both, 1 - side, keepdims=False)]
        )
    return x


def unfold(padded, step, rows, cols):
    windows = [
        padded[step * u : step * u + rows, step * q : step * q + cols, :]
        for u in range(3)
        for q in range(3)
    ]
    return jnp.concatenate(windows, axis=-1).reshape(rows * cols, -1)


def contract_rows(left, right):
    return lax.dot_general(
        left, right, (((0,), (0,)), ((), ())), preferred_element_type=jnp.float32
    )


def on_device(
    grid_feats, station_values, station_tile, station_cell, w_embed, w_first, w_second, cotangent
):
    cells = grid_feats[0]
    rows, cols, chans = cells.shape
    values = station_values[0]
    tiles = station_tile[0, :, 0]
    where = station_cell[0]
    n_tiles = lax.axis_size("row") * lax.axis_size("col")
    count = values.shape[0]
    capacity = max(2, 2 * count // n_tiles)
    slots = n_tiles * capacity
    hits = (tiles[:, None] == jnp.arange(n_tiles, dtype=jnp.int32)[None, :]).astype(jnp.int32)
    ranks = jnp.sum(jnp.cumsum(hits, axis=0) * hits, axis=1) - 1
    target = tiles * capacity + ranks
    chooser = (target[None, :] == jnp.arange(slots, dtype=jnp.int32)[:, None]).astype(jnp.bfloat16)
    chosen = jnp.dot(chooser, values, preferred_element_type=jnp.float32).astype(jnp.bfloat16)
    outgoing = jnp.dot(chosen, w_embed, preferred_element_type=jnp.float32)
    id_parts = jnp.zeros((count, chans), jnp.bfloat16)
    id_parts = id_parts.at[:, 0].set((where // 64 * 64).astype(jnp.bfloat16))
    id_parts = id_parts.at[:, 1].set((where % 64).astype(jnp.bfloat16))
    id_sums = jnp.dot(chooser, id_parts, preferred_element_type=jnp.float32)
    slot_ids = (id_sums[:, 0] + id_sums[:, 1]).reshape(n_tiles, capacity)
    id_row = jnp.zeros((n_tiles, 1, chans), jnp.float32).at[:, 0, :capacity].set(slot_ids)
    payload = jnp.concatenate([outgoing.reshape(n_tiles, capacity, chans), id_row], axis=1)
    arrived = lax.all_to_all(payload, ("row", "col"), split_axis=0, concat_axis=0, tiled=True)
    embedded = arrived[:, :capacity, :].reshape(slots, chans)
    arrived_ids = arrived[:, capacity, :capacity].reshape(slots)
    spread = (
        arrived_ids[None, :] == jnp.arange(rows * cols, dtype=jnp.float32)[:, None]
    ).astype(jnp.bfloat16)
    top = lax.reduce_precision(embedded, exponent_bits=8, mantissa_bits=7)
    rest = embedded - top
    middle = lax.reduce_precision(rest, exponent_bits=8, mantissa_bits=7)
    bottom = rest - middle
    split = jnp.concatenate([top, middle, bottom], axis=1).astype(jnp.bfloat16)
    pieces = jnp.dot(spread, split, preferred_element_type=jnp.float32)
    placed = pieces[:, :chans] + pieces[:, chans : 2 * chans] + pieces[:, 2 * chans :]
    first_in = (
        (cells.astype(jnp.float32).reshape(rows * cols, chans) + placed)
        .astype(jnp.bfloat16)
        .reshape(rows, cols, chans)
    )
    w_one = w_first.reshape(9 * chans, chans)
    w_two = w_second.reshape(9 * chans, chans)
    deep = with_halo(first_in, 3)
    pre_wide = jnp.dot(
        unfold(deep, 1, rows + 4, cols + 4), w_one, preferred_element_type=jnp.float32
    ).reshape(rows + 4, cols + 4, chans)
    row_ids = lax.axis_index("row") * rows - 2 + jnp.arange(rows + 4, dtype=jnp.int32)
    col_ids = lax.axis_index("col") * cols - 2 + jnp.arange(cols + 4, dtype=jnp.int32)
    inside_rows = (row_ids >= 0) & (row_ids < rows * lax.axis_size("row"))
    inside_cols = (col_ids >= 0) & (col_ids < cols * lax.axis_size("col"))
    inside = inside_rows[:, None] & inside_cols[None, :]
    padded1 = jnp.where(inside[:, :, None], jax.nn.silu(pre_wide), 0.0).astype(jnp.bfloat16)
    pre1 = pre_wide[2:-2, 2:-2].reshape(rows * cols, chans)
    act1 = padded1[2:-2, 2:-2]
    patches0 = unfold(deep[2:-2, 2:-2], 1, rows, cols)
    patches1 = unfold(padded1, 2, rows, cols)
    pre2 = jnp.dot(patches1, w_two, preferred_element_type=jnp.float32)
    output = (
        (act1.astype(jnp.float32).reshape(rows * cols, chans) + pre2)
        .astype(jnp.bfloat16)
        .reshape(1, rows, cols, chans)
    )
    back = cotangent[0]
    padded_back = with_halo(back, 2)
    w_turned = jnp.transpose(w_second[::-1, ::-1], (0, 1, 3, 2)).reshape(9 * chans, chans)
    back_flat = back.reshape(rows * cols, chans)
    grad_act1 = back_flat.astype(jnp.float32) + jnp.dot(
        unfold(padded_back, 2, rows, cols), w_turned, preferred_element_type=jnp.float32
    )
    sigmoid_pre = jax.nn.sigmoid(pre1)
    grad_pre1 = (grad_act1 * sigmoid_pre * (1.0 + pre1 * (1.0 - sigmoid_pre))).astype(jnp.bfloat16)
    grad_pre1 = lax.optimization_barrier(grad_pre1)
    first_term = contract_rows(patches0, grad_pre1)
    second_term = contract_rows(patches1, back_flat)
    first_sum, second_sum = jnp.split(tree_sum(jnp.concatenate([first_term, second_term])), 2)
    total_cells = (
        rows
        * lax.axis_size("row")
        * cols
        * lax.axis_size("col")
        * lax.axis_size("batch")
        * cells_per_sample_factor(grid_feats)
    )
    scale = 1.0 / math.sqrt(total_cells)
    grad_first = (first_sum * scale).reshape(3, 3, chans, chans)
    grad_second = (second_sum * scale).reshape(3, 3, chans, chans)
    return (output, grad_first, grad_second)


def cells_per_sample_factor(grid_feats):
    return grid_feats.shape[0]


def solution(mesh):
    return jax.shard_map(
        on_device,
        mesh=mesh,
        in_specs=(
            P("batch", "row", "col", None),
            P("batch", ("row", "col"), None),
            P("batch", ("row", "col"), None),
            P("batch", ("row", "col")),
            P(),
            P(),
            P(),
            P("batch", "row", "col", None),
        ),
        out_specs=(P("batch", "row", "col", None), P(), P()),
        check_vma=False,
    )
```

```python
import math

import jax
import jax.numpy as jnp
from jax import lax
from jax.sharding import PartitionSpec as P


def with_halo(array, sides, width):
    for axis, dim in sides:
        count, length = (lax.axis_size(axis), array.shape[dim])
        up = [(i, (i + 1) % count) for i in range(count - 1)]
        down = [(j, i) for i, j in up]
        last = lax.slice_in_dim(array, length - width, length, axis=dim)
        leading = lax.slice_in_dim(array, 0, width, axis=dim)
        before = lax.ppermute(last, axis, up)
        after = lax.ppermute(leading, axis, down)
        array = jnp.concatenate([before, array, after], axis=dim)
    return array


def halving_steps():
    steps = [("batch", 1)]
    for axis in ("row", "col"):
        d = 1
        while d < lax.axis_size(axis):
            steps.append((axis, d))
            d *= 2
    d = 2
    while d < lax.axis_size("batch"):
        steps.append(("batch", d))
        d *= 2
    return steps


def tree_sum(x, rider):
    steps = halving_steps()
    for step, (axis, d) in enumerate(steps):
        if step == 2:
            x, rider = lax.optimization_barrier((x, rider))
        pairs = [(i, i ^ d) for i in range(lax.axis_size(axis))]
        upper = (lax.axis_index(axis) // d) % 2 == 1
        half = x.shape[0] // 2
        side = upper.astype(jnp.int32)
        kept = lax.dynamic_slice_in_dim(x, side * half, half)
        sent = lax.dynamic_slice_in_dim(x, (1 - side) * half, half)
        x = kept + lax.ppermute(sent, axis, pairs)
    for axis, d in steps[::-1]:
        pairs = [(i, i ^ d) for i in range(lax.axis_size(axis))]
        upper = (lax.axis_index(axis) // d) % 2 == 1
        got = lax.ppermute(x, axis, pairs)
        both = jnp.stack([x, got])
        side = upper.astype(jnp.int32)
        x = jnp.concatenate(
            [lax.dynamic_index_in_dim(both, side, keepdims=False),
             lax.dynamic_index_in_dim(both, 1 - side, keepdims=False)]
        )
    return x, rider


def unfold(padded, step, rows, cols):
    windows = [
        padded[step * u : step * u + rows, step * q : step * q + cols, :]
        for u in range(3)
        for q in range(3)
    ]
    return jnp.concatenate(windows, axis=-1).reshape(rows * cols, -1)


def contract_rows(left, right):
    return lax.dot_general(
        left, right, (((0,), (0,)), ((), ())), preferred_element_type=jnp.float32
    )


def on_device(
    grid_feats, station_values, station_tile, station_cell, w_embed, w_first, w_second, cotangent
):
    cells = grid_feats[0]
    rows, cols, chans = cells.shape
    values = station_values[0]
    tiles = station_tile[0, :, 0]
    where = station_cell[0]
    n_tiles = lax.axis_size("row") * lax.axis_size("col")
    count = values.shape[0]
    capacity = max(2, 2 * count // n_tiles)
    slots = n_tiles * capacity
    hits = (tiles[:, None] == jnp.arange(n_tiles, dtype=jnp.int32)[None, :]).astype(jnp.int32)
    ranks = jnp.sum(jnp.cumsum(hits, axis=0) * hits, axis=1) - 1
    target = tiles * capacity + ranks
    chooser = (target[None, :] == jnp.arange(slots, dtype=jnp.int32)[:, None]).astype(jnp.bfloat16)
    chosen = jnp.dot(chooser, values, preferred_element_type=jnp.float32).astype(jnp.bfloat16)
    outgoing = jnp.dot(chosen, w_embed, preferred_element_type=jnp.float32)
    id_parts = jnp.zeros((count, chans), jnp.bfloat16)
    id_parts = id_parts.at[:, 0].set((where // 64 * 64).astype(jnp.bfloat16))
    id_parts = id_parts.at[:, 1].set((where % 64).astype(jnp.bfloat16))
    id_sums = jnp.dot(chooser, id_parts, preferred_element_type=jnp.float32)
    slot_ids = (id_sums[:, 0] + id_sums[:, 1]).reshape(n_tiles, capacity)
    id_row = jnp.zeros((n_tiles, 1, chans), jnp.float32).at[:, 0, :capacity].set(slot_ids)
    payload = jnp.concatenate([outgoing.reshape(n_tiles, capacity, chans), id_row], axis=1)
    arrived = lax.all_to_all(payload, ("row", "col"), split_axis=0, concat_axis=0, tiled=True)
    embedded = arrived[:, :capacity, :].reshape(slots, chans)
    arrived_ids = arrived[:, capacity, :capacity].reshape(slots)
    spread = (
        arrived_ids[None, :] == jnp.arange(rows * cols, dtype=jnp.float32)[:, None]
    ).astype(jnp.bfloat16)
    top = lax.reduce_precision(embedded, exponent_bits=8, mantissa_bits=7)
    rest = embedded - top
    middle = lax.reduce_precision(rest, exponent_bits=8, mantissa_bits=7)
    bottom = rest - middle
    split = jnp.concatenate([top, middle, bottom], axis=1).astype(jnp.bfloat16)
    pieces = jnp.dot(spread, split, preferred_element_type=jnp.float32)
    placed = pieces[:, :chans] + pieces[:, chans : 2 * chans] + pieces[:, 2 * chans :]
    first_in = (
        (cells.astype(jnp.float32).reshape(rows * cols, chans) + placed)
        .astype(jnp.bfloat16)
        .reshape(rows, cols, chans)
    )
    w_one = w_first.reshape(9 * chans, chans)
    w_two = w_second.reshape(9 * chans, chans)
    deep = with_halo(first_in, (("row", 0), ("col", 1)), 3)
    pre_wide = jnp.dot(
        unfold(deep, 1, rows + 4, cols + 4), w_one, preferred_element_type=jnp.float32
    ).reshape(rows + 4, cols + 4, chans)
    row_ids = lax.axis_index("row") * rows - 2 + jnp.arange(rows + 4, dtype=jnp.int32)
    col_ids = lax.axis_index("col") * cols - 2 + jnp.arange(cols + 4, dtype=jnp.int32)
    inside_rows = (row_ids >= 0) & (row_ids < rows * lax.axis_size("row"))
    inside_cols = (col_ids >= 0) & (col_ids < cols * lax.axis_size("col"))
    inside = inside_rows[:, None] & inside_cols[None, :]
    padded1 = jnp.where(inside[:, :, None], jax.nn.silu(pre_wide), 0.0).astype(jnp.bfloat16)
    pre1 = pre_wide[2:-2, 2:-2].reshape(rows * cols, chans)
    act1 = padded1[2:-2, 2:-2]
    patches0 = unfold(deep[2:-2, 2:-2], 1, rows, cols)
    patches1 = unfold(padded1, 2, rows, cols)
    back = cotangent[0]
    padded_back = with_halo(back, (("row", 0), ("col", 1)), 2)
    w_turned = jnp.transpose(w_second[::-1, ::-1], (0, 1, 3, 2)).reshape(9 * chans, chans)
    back_flat = back.reshape(rows * cols, chans)
    grad_act1 = back_flat.astype(jnp.float32) + jnp.dot(
        unfold(padded_back, 2, rows, cols), w_turned, preferred_element_type=jnp.float32
    )
    sigmoid_pre = jax.nn.sigmoid(pre1)
    grad_pre1 = (grad_act1 * sigmoid_pre * (1.0 + pre1 * (1.0 - sigmoid_pre))).astype(jnp.bfloat16)
    grad_pre1 = lax.optimization_barrier(grad_pre1)
    first_term = contract_rows(patches0, grad_pre1)
    second_term = contract_rows(patches1, back_flat)
    total_cells = (
        rows
        * lax.axis_size("row")
        * cols
        * lax.axis_size("col")
        * lax.axis_size("batch")
        * cells_per_sample_factor(grid_feats)
    )
    scale = 1.0 / math.sqrt(total_cells)
    terms = jnp.concatenate([first_term, second_term]) * scale
    pre2 = jnp.dot(patches1, w_two, preferred_element_type=jnp.float32)
    output = (
        (act1.astype(jnp.float32).reshape(rows * cols, chans) + pre2)
        .astype(jnp.bfloat16)
        .reshape(1, rows, cols, chans)
    )
    summed, output = tree_sum(terms, output)
    first_sum, second_sum = jnp.split(summed, 2)
    grad_first = first_sum.reshape(3, 3, chans, chans)
    grad_second = second_sum.reshape(3, 3, chans, chans)
    return (output, grad_first, grad_second)


def cells_per_sample_factor(grid_feats):
    return grid_feats.shape[0]


def solution(mesh):
    return jax.shard_map(
        on_device,
        mesh=mesh,
        in_specs=(
            P("batch", "row", "col", None),
            P("batch", ("row", "col"), None),
            P("batch", ("row", "col"), None),
            P("batch", ("row", "col")),
            P(),
            P(),
            P(),
            P("batch", "row", "col", None),
        ),
        out_specs=(P("batch", "row", "col", None), P(), P()),
        check_vma=False,
    )
```

```python
import math

import jax
import jax.numpy as jnp
from jax import lax
from jax.sharding import PartitionSpec as P


def with_halo(array, sides, width):
    for axis, dim in sides:
        count, length = (lax.axis_size(axis), array.shape[dim])
        up = [(i, (i + 1) % count) for i in range(count - 1)]
        down = [(j, i) for i, j in up]
        last = lax.slice_in_dim(array, length - width, length, axis=dim)
        leading = lax.slice_in_dim(array, 0, width, axis=dim)
        before = lax.ppermute(last, axis, up)
        after = lax.ppermute(leading, axis, down)
        array = jnp.concatenate([before, array, after], axis=dim)
    return array


def halving_steps():
    steps = [("batch", 1)]
    for axis in ("row", "col"):
        d = 1
        while d < lax.axis_size(axis):
            steps.append((axis, d))
            d *= 2
    d = 2
    while d < lax.axis_size("batch"):
        steps.append(("batch", d))
        d *= 2
    return steps


def tree_sum(x, rider):
    steps = halving_steps()
    for step, (axis, d) in enumerate(steps):
        if step == 2:
            x, rider = lax.optimization_barrier((x, rider))
        pairs = [(i, i ^ d) for i in range(lax.axis_size(axis))]
        upper = (lax.axis_index(axis) // d) % 2 == 1
        half = x.shape[0] // 2
        side = upper.astype(jnp.int32)
        kept = lax.dynamic_slice_in_dim(x, side * half, half)
        sent = lax.dynamic_slice_in_dim(x, (1 - side) * half, half)
        x = kept + lax.ppermute(sent, axis, pairs)
    for axis, d in steps[::-1]:
        pairs = [(i, i ^ d) for i in range(lax.axis_size(axis))]
        upper = (lax.axis_index(axis) // d) % 2 == 1
        got = lax.ppermute(x, axis, pairs)
        both = jnp.stack([x, got])
        side = upper.astype(jnp.int32)
        x = jnp.concatenate(
            [lax.dynamic_index_in_dim(both, side, keepdims=False),
             lax.dynamic_index_in_dim(both, 1 - side, keepdims=False)]
        )
    return x, rider


def unfold(padded, step, rows, cols):
    windows = [
        padded[step * u : step * u + rows, step * q : step * q + cols, :]
        for u in range(3)
        for q in range(3)
    ]
    return jnp.concatenate(windows, axis=-1).reshape(rows * cols, -1)


def contract_rows(left, right):
    return lax.dot_general(
        left, right, (((0,), (0,)), ((), ())), preferred_element_type=jnp.float32
    )


def on_device(
    grid_feats, station_values, station_tile, station_cell, w_embed, w_first, w_second, cotangent
):
    cells = grid_feats[0]
    rows, cols, chans = cells.shape
    values = station_values[0]
    tiles = station_tile[0, :, 0]
    where = station_cell[0]
    n_tiles = lax.axis_size("row") * lax.axis_size("col")
    count = values.shape[0]
    capacity = max(2, 2 * count // n_tiles)
    slots = n_tiles * capacity
    hits = (tiles[:, None] == jnp.arange(n_tiles, dtype=jnp.int32)[None, :]).astype(jnp.int32)
    ranks = jnp.sum(jnp.cumsum(hits, axis=0) * hits, axis=1) - 1
    target = tiles * capacity + ranks
    chooser = (target[None, :] == jnp.arange(slots, dtype=jnp.int32)[:, None]).astype(jnp.bfloat16)
    chosen = jnp.dot(chooser, values, preferred_element_type=jnp.float32).astype(jnp.bfloat16)
    outgoing = jnp.dot(chosen, w_embed, preferred_element_type=jnp.float32)
    id_parts = jnp.zeros((count, chans), jnp.bfloat16)
    id_parts = id_parts.at[:, 0].set((where // 64 * 64).astype(jnp.bfloat16))
    id_parts = id_parts.at[:, 1].set((where % 64).astype(jnp.bfloat16))
    id_sums = jnp.dot(chooser, id_parts, preferred_element_type=jnp.float32)
    slot_ids = (id_sums[:, 0] + id_sums[:, 1]).reshape(n_tiles, capacity)
    id_row = jnp.zeros((n_tiles, 1, chans), jnp.float32).at[:, 0, :capacity].set(slot_ids)
    payload = jnp.concatenate([outgoing.reshape(n_tiles, capacity, chans), id_row], axis=1)
    arrived = lax.all_to_all(payload, ("row", "col"), split_axis=0, concat_axis=0, tiled=True)
    embedded = arrived[:, :capacity, :].reshape(slots, chans)
    arrived_ids = arrived[:, capacity, :capacity].reshape(slots)
    spread = (
        arrived_ids[None, :] == jnp.arange(rows * cols, dtype=jnp.float32)[:, None]
    ).astype(jnp.bfloat16)
    top = lax.reduce_precision(embedded, exponent_bits=8, mantissa_bits=7)
    rest = embedded - top
    middle = lax.reduce_precision(rest, exponent_bits=8, mantissa_bits=7)
    bottom = rest - middle
    split = jnp.concatenate([top, middle, bottom], axis=1).astype(jnp.bfloat16)
    pieces = jnp.dot(spread, split, preferred_element_type=jnp.float32)
    placed = pieces[:, :chans] + pieces[:, chans : 2 * chans] + pieces[:, 2 * chans :]
    first_in = (
        (cells.astype(jnp.float32).reshape(rows * cols, chans) + placed)
        .astype(jnp.bfloat16)
        .reshape(rows, cols, chans)
    )
    w_one = w_first.reshape(9 * chans, chans)
    w_two = w_second.reshape(9 * chans, chans)
    back = cotangent[0]
    padded_back = with_halo(back, (("row", 0), ("col", 1)), 2)
    w_turned = jnp.transpose(w_second[::-1, ::-1], (0, 1, 3, 2)).reshape(9 * chans, chans)
    back_flat = back.reshape(rows * cols, chans)
    grad_act1 = back_flat.astype(jnp.float32) + jnp.dot(
        unfold(padded_back, 2, rows, cols), w_turned, preferred_element_type=jnp.float32
    )
    deep = with_halo(first_in, (("row", 0), ("col", 1)), 3)
    deep, grad_act1 = lax.optimization_barrier((deep, grad_act1))
    pre_wide = jnp.dot(
        unfold(deep, 1, rows + 4, cols + 4), w_one, preferred_element_type=jnp.float32
    ).reshape(rows + 4, cols + 4, chans)
    row_ids = lax.axis_index("row") * rows - 2 + jnp.arange(rows + 4, dtype=jnp.int32)
    col_ids = lax.axis_index("col") * cols - 2 + jnp.arange(cols + 4, dtype=jnp.int32)
    inside_rows = (row_ids >= 0) & (row_ids < rows * lax.axis_size("row"))
    inside_cols = (col_ids >= 0) & (col_ids < cols * lax.axis_size("col"))
    inside = inside_rows[:, None] & inside_cols[None, :]
    padded1 = jnp.where(inside[:, :, None], jax.nn.silu(pre_wide), 0.0).astype(jnp.bfloat16)
    pre1 = pre_wide[2:-2, 2:-2].reshape(rows * cols, chans)
    act1 = padded1[2:-2, 2:-2]
    patches0 = unfold(deep[2:-2, 2:-2], 1, rows, cols)
    patches1 = unfold(padded1, 2, rows, cols)
    sigmoid_pre = jax.nn.sigmoid(pre1)
    grad_pre1 = (grad_act1 * sigmoid_pre * (1.0 + pre1 * (1.0 - sigmoid_pre))).astype(jnp.bfloat16)
    grad_pre1 = lax.optimization_barrier(grad_pre1)
    first_term = contract_rows(patches0, grad_pre1)
    second_term = contract_rows(patches1, back_flat)
    total_cells = (
        rows
        * lax.axis_size("row")
        * cols
        * lax.axis_size("col")
        * lax.axis_size("batch")
        * cells_per_sample_factor(grid_feats)
    )
    scale = 1.0 / math.sqrt(total_cells)
    terms = jnp.concatenate([first_term, second_term]) * scale
    pre2 = jnp.dot(patches1, w_two, preferred_element_type=jnp.float32)
    output = (
        (act1.astype(jnp.float32).reshape(rows * cols, chans) + pre2)
        .astype(jnp.bfloat16)
        .reshape(1, rows, cols, chans)
    )
    summed, output = tree_sum(terms, output)
    first_sum, second_sum = jnp.split(summed, 2)
    grad_first = first_sum.reshape(3, 3, chans, chans)
    grad_second = second_sum.reshape(3, 3, chans, chans)
    return (output, grad_first, grad_second)


def cells_per_sample_factor(grid_feats):
    return grid_feats.shape[0]


def solution(mesh):
    return jax.shard_map(
        on_device,
        mesh=mesh,
        in_specs=(
            P("batch", "row", "col", None),
            P("batch", ("row", "col"), None),
            P("batch", ("row", "col"), None),
            P("batch", ("row", "col")),
            P(),
            P(),
            P(),
            P("batch", "row", "col", None),
        ),
        out_specs=(P("batch", "row", "col", None), P(), P()),
        check_vma=False,
    )
```

```python
import math

import jax
import jax.numpy as jnp
from jax import lax
from jax.sharding import PartitionSpec as P


def with_halo(array, sides, width):
    for axis, dim in sides:
        count, length = (lax.axis_size(axis), array.shape[dim])
        up = [(i, (i + 1) % count) for i in range(count - 1)]
        down = [(j, i) for i, j in up]
        last = lax.slice_in_dim(array, length - width, length, axis=dim)
        leading = lax.slice_in_dim(array, 0, width, axis=dim)
        before = lax.ppermute(last, axis, up)
        after = lax.ppermute(leading, axis, down)
        array = jnp.concatenate([before, array, after], axis=dim)
    return array


def halving_steps():
    steps = [("batch", 1)]
    d = 1
    while d < lax.axis_size("row"):
        steps.append(("row", d))
        d *= 2
    d = 2
    while d < lax.axis_size("batch"):
        steps.append(("batch", d))
        d *= 2
    return steps


def tree_sum(x, rider):
    steps = halving_steps()
    for step, (axis, d) in enumerate(steps):
        if step == 2:
            x, rider = lax.optimization_barrier((x, rider))
        pairs = [(i, i ^ d) for i in range(lax.axis_size(axis))]
        upper = (lax.axis_index(axis) // d) % 2 == 1
        half = x.shape[0] // 2
        side = upper.astype(jnp.int32)
        kept = lax.dynamic_slice_in_dim(x, side * half, half)
        sent = lax.dynamic_slice_in_dim(x, (1 - side) * half, half)
        x = kept + lax.ppermute(sent, axis, pairs)
    spread_over = lax.axis_size("col")
    parts = x.reshape(spread_over, x.shape[0] // spread_over, x.shape[1])
    x = lax.all_to_all(parts, "col", 0, 0, tiled=True).sum(0)
    copies = jnp.broadcast_to(x[None], (spread_over,) + x.shape)
    x = lax.all_to_all(copies, "col", 0, 0, tiled=True).reshape(-1, x.shape[1])
    for axis, d in steps[::-1]:
        pairs = [(i, i ^ d) for i in range(lax.axis_size(axis))]
        upper = (lax.axis_index(axis) // d) % 2 == 1
        got = lax.ppermute(x, axis, pairs)
        both = jnp.stack([x, got])
        side = upper.astype(jnp.int32)
        x = jnp.concatenate(
            [lax.dynamic_index_in_dim(both, side, keepdims=False),
             lax.dynamic_index_in_dim(both, 1 - side, keepdims=False)]
        )
    return x, rider


def unfold(padded, step, rows, cols):
    windows = [
        padded[step * u : step * u + rows, step * q : step * q + cols, :]
        for u in range(3)
        for q in range(3)
    ]
    return jnp.concatenate(windows, axis=-1).reshape(rows * cols, -1)


def contract_rows(left, right):
    return lax.dot_general(
        left, right, (((0,), (0,)), ((), ())), preferred_element_type=jnp.float32
    )


def on_device(
    grid_feats, station_values, station_tile, station_cell, w_embed, w_first, w_second, cotangent
):
    cells = grid_feats[0]
    rows, cols, chans = cells.shape
    values = station_values[0]
    tiles = station_tile[0, :, 0]
    where = station_cell[0]
    n_tiles = lax.axis_size("row") * lax.axis_size("col")
    count = values.shape[0]
    capacity = max(2, 2 * count // n_tiles)
    slots = n_tiles * capacity
    hits = (tiles[:, None] == jnp.arange(n_tiles, dtype=jnp.int32)[None, :]).astype(jnp.int32)
    ranks = jnp.sum(jnp.cumsum(hits, axis=0) * hits, axis=1) - 1
    target = tiles * capacity + ranks
    chooser = (target[None, :] == jnp.arange(slots, dtype=jnp.int32)[:, None]).astype(jnp.bfloat16)
    chosen = jnp.dot(chooser, values, preferred_element_type=jnp.float32).astype(jnp.bfloat16)
    outgoing = jnp.dot(chosen, w_embed, preferred_element_type=jnp.float32)
    id_parts = jnp.zeros((count, chans), jnp.bfloat16)
    id_parts = id_parts.at[:, 0].set((where // 64 * 64).astype(jnp.bfloat16))
    id_parts = id_parts.at[:, 1].set((where % 64).astype(jnp.bfloat16))
    id_sums = jnp.dot(chooser, id_parts, preferred_element_type=jnp.float32)
    slot_ids = (id_sums[:, 0] + id_sums[:, 1]).reshape(n_tiles, capacity)
    id_row = jnp.zeros((n_tiles, 1, chans), jnp.float32).at[:, 0, :capacity].set(slot_ids)
    payload = jnp.concatenate([outgoing.reshape(n_tiles, capacity, chans), id_row], axis=1)
    arrived = lax.all_to_all(payload, ("row", "col"), split_axis=0, concat_axis=0, tiled=True)
    embedded = arrived[:, :capacity, :].reshape(slots, chans)
    arrived_ids = arrived[:, capacity, :capacity].reshape(slots)
    spread = (
        arrived_ids[None, :] == jnp.arange(rows * cols, dtype=jnp.float32)[:, None]
    ).astype(jnp.bfloat16)
    top = lax.reduce_precision(embedded, exponent_bits=8, mantissa_bits=7)
    rest = embedded - top
    middle = lax.reduce_precision(rest, exponent_bits=8, mantissa_bits=7)
    bottom = rest - middle
    split = jnp.concatenate([top, middle, bottom], axis=1).astype(jnp.bfloat16)
    pieces = jnp.dot(spread, split, preferred_element_type=jnp.float32)
    placed = pieces[:, :chans] + pieces[:, chans : 2 * chans] + pieces[:, 2 * chans :]
    first_in = (
        (cells.astype(jnp.float32).reshape(rows * cols, chans) + placed)
        .astype(jnp.bfloat16)
        .reshape(rows, cols, chans)
    )
    w_one = w_first.reshape(9 * chans, chans)
    w_two = w_second.reshape(9 * chans, chans)
    back = cotangent[0]
    padded_back = with_halo(back, (("row", 0), ("col", 1)), 2)
    w_turned = jnp.transpose(w_second[::-1, ::-1], (0, 1, 3, 2)).reshape(9 * chans, chans)
    back_flat = back.reshape(rows * cols, chans)
    grad_act1 = back_flat.astype(jnp.float32) + jnp.dot(
        unfold(padded_back, 2, rows, cols), w_turned, preferred_element_type=jnp.float32
    )
    deep = with_halo(first_in, (("row", 0), ("col", 1)), 3)
    deep, grad_act1 = lax.optimization_barrier((deep, grad_act1))
    pre_wide = jnp.dot(
        unfold(deep, 1, rows + 4, cols + 4), w_one, preferred_element_type=jnp.float32
    ).reshape(rows + 4, cols + 4, chans)
    row_ids = lax.axis_index("row") * rows - 2 + jnp.arange(rows + 4, dtype=jnp.int32)
    col_ids = lax.axis_index("col") * cols - 2 + jnp.arange(cols + 4, dtype=jnp.int32)
    inside_rows = (row_ids >= 0) & (row_ids < rows * lax.axis_size("row"))
    inside_cols = (col_ids >= 0) & (col_ids < cols * lax.axis_size("col"))
    inside = inside_rows[:, None] & inside_cols[None, :]
    padded1 = jnp.where(inside[:, :, None], jax.nn.silu(pre_wide), 0.0).astype(jnp.bfloat16)
    pre1 = pre_wide[2:-2, 2:-2].reshape(rows * cols, chans)
    act1 = padded1[2:-2, 2:-2]
    patches0 = unfold(deep[2:-2, 2:-2], 1, rows, cols)
    patches1 = unfold(padded1, 2, rows, cols)
    sigmoid_pre = jax.nn.sigmoid(pre1)
    grad_pre1 = (grad_act1 * sigmoid_pre * (1.0 + pre1 * (1.0 - sigmoid_pre))).astype(jnp.bfloat16)
    grad_pre1 = lax.optimization_barrier(grad_pre1)
    first_term = contract_rows(patches0, grad_pre1)
    second_term = contract_rows(patches1, back_flat)
    total_cells = (
        rows
        * lax.axis_size("row")
        * cols
        * lax.axis_size("col")
        * lax.axis_size("batch")
        * cells_per_sample_factor(grid_feats)
    )
    scale = 1.0 / math.sqrt(total_cells)
    terms = jnp.concatenate([first_term, second_term]) * scale
    pre2 = jnp.dot(patches1, w_two, preferred_element_type=jnp.float32)
    output = (
        (act1.astype(jnp.float32).reshape(rows * cols, chans) + pre2)
        .astype(jnp.bfloat16)
        .reshape(1, rows, cols, chans)
    )
    summed, output = tree_sum(terms, output)
    first_sum, second_sum = jnp.split(summed, 2)
    grad_first = first_sum.reshape(3, 3, chans, chans)
    grad_second = second_sum.reshape(3, 3, chans, chans)
    return (output, grad_first, grad_second)


def cells_per_sample_factor(grid_feats):
    return grid_feats.shape[0]


def solution(mesh):
    return jax.shard_map(
        on_device,
        mesh=mesh,
        in_specs=(
            P("batch", "row", "col", None),
            P("batch", ("row", "col"), None),
            P("batch", ("row", "col"), None),
            P("batch", ("row", "col")),
            P(),
            P(),
            P(),
            P("batch", "row", "col", None),
        ),
        out_specs=(P("batch", "row", "col", None), P(), P()),
        check_vma=False,
    )
```

```python
import math

import jax
import jax.numpy as jnp
from jax import lax
from jax.sharding import PartitionSpec as P


def with_halo(array, sides, width):
    for axis, dim in sides:
        count, length = (lax.axis_size(axis), array.shape[dim])
        up = [(i, (i + 1) % count) for i in range(count - 1)]
        down = [(j, i) for i, j in up]
        last = lax.slice_in_dim(array, length - width, length, axis=dim)
        leading = lax.slice_in_dim(array, 0, width, axis=dim)
        before = lax.ppermute(last, axis, up)
        after = lax.ppermute(leading, axis, down)
        array = jnp.concatenate([before, array, after], axis=dim)
    return array


def halving_stages():
    stages = [("batch", 1), ("row", 0)]
    d = 2
    while d < lax.axis_size("batch"):
        stages.append(("batch", d))
        d *= 2
    return stages + [("col", 0)]


def tree_sum(x, rider):
    stages = halving_stages()
    for stage, (axis, d) in enumerate(stages):
        if stage == 2:
            x, rider = lax.optimization_barrier((x, rider))
        if d == 0:
            n = lax.axis_size(axis)
            parts = x.reshape(n, x.shape[0] // n, x.shape[1])
            x = lax.all_to_all(parts, axis, 0, 0, tiled=True).sum(0)
            continue
        pairs = [(i, i ^ d) for i in range(lax.axis_size(axis))]
        upper = (lax.axis_index(axis) // d) % 2 == 1
        half = x.shape[0] // 2
        side = upper.astype(jnp.int32)
        kept = lax.dynamic_slice_in_dim(x, side * half, half)
        sent = lax.dynamic_slice_in_dim(x, (1 - side) * half, half)
        x = kept + lax.ppermute(sent, axis, pairs)
    for axis, d in stages[::-1]:
        if d == 0:
            n = lax.axis_size(axis)
            copies = jnp.broadcast_to(x[None], (n,) + x.shape)
            x = lax.all_to_all(copies, axis, 0, 0, tiled=True).reshape(-1, x.shape[1])
            continue
        pairs = [(i, i ^ d) for i in range(lax.axis_size(axis))]
        upper = (lax.axis_index(axis) // d) % 2 == 1
        got = lax.ppermute(x, axis, pairs)
        both = jnp.stack([x, got])
        side = upper.astype(jnp.int32)
        x = jnp.concatenate(
            [lax.dynamic_index_in_dim(both, side, keepdims=False),
             lax.dynamic_index_in_dim(both, 1 - side, keepdims=False)]
        )
    return x, rider


def unfold(padded, step, rows, cols):
    windows = [
        padded[step * u : step * u + rows, step * q : step * q + cols, :]
        for u in range(3)
        for q in range(3)
    ]
    return jnp.concatenate(windows, axis=-1).reshape(rows * cols, -1)


def contract_rows(left, right):
    return lax.dot_general(
        left, right, (((0,), (0,)), ((), ())), preferred_element_type=jnp.float32
    )


def on_device(
    grid_feats, station_values, station_tile, station_cell, w_embed, w_first, w_second, cotangent
):
    cells = grid_feats[0]
    rows, cols, chans = cells.shape
    values = station_values[0]
    tiles = station_tile[0, :, 0]
    where = station_cell[0]
    n_tiles = lax.axis_size("row") * lax.axis_size("col")
    count = values.shape[0]
    capacity = max(2, 2 * count // n_tiles)
    slots = n_tiles * capacity
    hits = (tiles[:, None] == jnp.arange(n_tiles, dtype=jnp.int32)[None, :]).astype(jnp.int32)
    ranks = jnp.sum(jnp.cumsum(hits, axis=0) * hits, axis=1) - 1
    target = tiles * capacity + ranks
    chooser = (target[None, :] == jnp.arange(slots, dtype=jnp.int32)[:, None]).astype(jnp.bfloat16)
    chosen = jnp.dot(chooser, values, preferred_element_type=jnp.float32).astype(jnp.bfloat16)
    outgoing = jnp.dot(chosen, w_embed, preferred_element_type=jnp.float32)
    id_parts = jnp.zeros((count, chans), jnp.bfloat16)
    id_parts = id_parts.at[:, 0].set((where // 64 * 64).astype(jnp.bfloat16))
    id_parts = id_parts.at[:, 1].set((where % 64).astype(jnp.bfloat16))
    id_sums = jnp.dot(chooser, id_parts, preferred_element_type=jnp.float32)
    slot_ids = (id_sums[:, 0] + id_sums[:, 1]).reshape(n_tiles, capacity)
    id_row = jnp.zeros((n_tiles, 1, chans), jnp.float32).at[:, 0, :capacity].set(slot_ids)
    payload = jnp.concatenate([outgoing.reshape(n_tiles, capacity, chans), id_row], axis=1)
    arrived = lax.all_to_all(payload, ("row", "col"), split_axis=0, concat_axis=0, tiled=True)
    embedded = arrived[:, :capacity, :].reshape(slots, chans)
    arrived_ids = arrived[:, capacity, :capacity].reshape(slots)
    spread = (
        arrived_ids[None, :] == jnp.arange(rows * cols, dtype=jnp.float32)[:, None]
    ).astype(jnp.bfloat16)
    top = lax.reduce_precision(embedded, exponent_bits=8, mantissa_bits=7)
    rest = embedded - top
    middle = lax.reduce_precision(rest, exponent_bits=8, mantissa_bits=7)
    bottom = rest - middle
    split = jnp.concatenate([top, middle, bottom], axis=1).astype(jnp.bfloat16)
    pieces = jnp.dot(spread, split, preferred_element_type=jnp.float32)
    placed = pieces[:, :chans] + pieces[:, chans : 2 * chans] + pieces[:, 2 * chans :]
    first_in = (
        (cells.astype(jnp.float32).reshape(rows * cols, chans) + placed)
        .astype(jnp.bfloat16)
        .reshape(rows, cols, chans)
    )
    w_one = w_first.reshape(9 * chans, chans)
    w_two = w_second.reshape(9 * chans, chans)
    back = cotangent[0]
    padded_back = with_halo(back, (("row", 0), ("col", 1)), 2)
    w_turned = jnp.transpose(w_second[::-1, ::-1], (0, 1, 3, 2)).reshape(9 * chans, chans)
    back_flat = back.reshape(rows * cols, chans)
    grad_act1 = back_flat.astype(jnp.float32) + jnp.dot(
        unfold(padded_back, 2, rows, cols), w_turned, preferred_element_type=jnp.float32
    )
    deep = with_halo(first_in, (("row", 0), ("col", 1)), 3)
    deep, grad_act1 = lax.optimization_barrier((deep, grad_act1))
    pre_wide = jnp.dot(
        unfold(deep, 1, rows + 4, cols + 4), w_one, preferred_element_type=jnp.float32
    ).reshape(rows + 4, cols + 4, chans)
    row_ids = lax.axis_index("row") * rows - 2 + jnp.arange(rows + 4, dtype=jnp.int32)
    col_ids = lax.axis_index("col") * cols - 2 + jnp.arange(cols + 4, dtype=jnp.int32)
    inside_rows = (row_ids >= 0) & (row_ids < rows * lax.axis_size("row"))
    inside_cols = (col_ids >= 0) & (col_ids < cols * lax.axis_size("col"))
    inside = inside_rows[:, None] & inside_cols[None, :]
    padded1 = jnp.where(inside[:, :, None], jax.nn.silu(pre_wide), 0.0).astype(jnp.bfloat16)
    pre1 = pre_wide[2:-2, 2:-2].reshape(rows * cols, chans)
    act1 = padded1[2:-2, 2:-2]
    patches0 = unfold(deep[2:-2, 2:-2], 1, rows, cols)
    patches1 = unfold(padded1, 2, rows, cols)
    sigmoid_pre = jax.nn.sigmoid(pre1)
    grad_pre1 = (grad_act1 * sigmoid_pre * (1.0 + pre1 * (1.0 - sigmoid_pre))).astype(jnp.bfloat16)
    grad_pre1 = lax.optimization_barrier(grad_pre1)
    first_term = contract_rows(patches0, grad_pre1)
    second_term = contract_rows(patches1, back_flat)
    total_cells = (
        rows
        * lax.axis_size("row")
        * cols
        * lax.axis_size("col")
        * lax.axis_size("batch")
        * cells_per_sample_factor(grid_feats)
    )
    scale = 1.0 / math.sqrt(total_cells)
    terms = jnp.concatenate([first_term, second_term]) * scale
    pre2 = jnp.dot(patches1, w_two, preferred_element_type=jnp.float32)
    output = (
        (act1.astype(jnp.float32).reshape(rows * cols, chans) + pre2)
        .astype(jnp.bfloat16)
        .reshape(1, rows, cols, chans)
    )
    summed, output = tree_sum(terms, output)
    first_sum, second_sum = jnp.split(summed, 2)
    grad_first = first_sum.reshape(3, 3, chans, chans)
    grad_second = second_sum.reshape(3, 3, chans, chans)
    return (output, grad_first, grad_second)


def cells_per_sample_factor(grid_feats):
    return grid_feats.shape[0]


def solution(mesh):
    return jax.shard_map(
        on_device,
        mesh=mesh,
        in_specs=(
            P("batch", "row", "col", None),
            P("batch", ("row", "col"), None),
            P("batch", ("row", "col"), None),
            P("batch", ("row", "col")),
            P(),
            P(),
            P(),
            P("batch", "row", "col", None),
        ),
        out_specs=(P("batch", "row", "col", None), P(), P()),
        check_vma=False,
    )
```

```python
import math

import jax
import jax.numpy as jnp
from jax import lax
from jax.sharding import PartitionSpec as P


def with_halo(array, sides, width):
    for axis, dim in sides:
        count, length = (lax.axis_size(axis), array.shape[dim])
        up = [(i, (i + 1) % count) for i in range(count - 1)]
        down = [(j, i) for i, j in up]
        last = lax.slice_in_dim(array, length - width, length, axis=dim)
        leading = lax.slice_in_dim(array, 0, width, axis=dim)
        before = lax.ppermute(last, axis, up)
        after = lax.ppermute(leading, axis, down)
        array = jnp.concatenate([before, array, after], axis=dim)
    return array


def halving_steps():
    steps = []
    for axis in ("batch", "row"):
        d = 1
        while d < lax.axis_size(axis):
            steps.append((axis, d))
            d *= 2
    return steps


def tree_sum(x, rider):
    steps = halving_steps()
    for step, (axis, d) in enumerate(steps):
        if step == 2:
            x, rider = lax.optimization_barrier((x, rider))
        pairs = [(i, i ^ d) for i in range(lax.axis_size(axis))]
        upper = (lax.axis_index(axis) // d) % 2 == 1
        half = x.shape[0] // 2
        side = upper.astype(jnp.int32)
        kept = lax.dynamic_slice_in_dim(x, side * half, half)
        sent = lax.dynamic_slice_in_dim(x, (1 - side) * half, half)
        x = kept + lax.ppermute(sent, axis, pairs)
    spread_over = lax.axis_size("col")
    parts = x.reshape(spread_over, x.shape[0] // spread_over, x.shape[1])
    x = lax.all_to_all(parts, "col", 0, 0, tiled=True).sum(0)
    copies = jnp.broadcast_to(x[None], (spread_over,) + x.shape)
    x = lax.all_to_all(copies, "col", 0, 0, tiled=True).reshape(-1, x.shape[1])
    for axis, d in steps[::-1]:
        pairs = [(i, i ^ d) for i in range(lax.axis_size(axis))]
        upper = (lax.axis_index(axis) // d) % 2 == 1
        got = lax.ppermute(x, axis, pairs)
        both = jnp.stack([x, got])
        side = upper.astype(jnp.int32)
        x = jnp.concatenate(
            [lax.dynamic_index_in_dim(both, side, keepdims=False),
             lax.dynamic_index_in_dim(both, 1 - side, keepdims=False)]
        )
    return x, rider


def unfold(padded, step, rows, cols):
    windows = [
        padded[step * u : step * u + rows, step * q : step * q + cols, :]
        for u in range(3)
        for q in range(3)
    ]
    return jnp.concatenate(windows, axis=-1).reshape(rows * cols, -1)


def contract_rows(left, right):
    return lax.dot_general(
        left, right, (((0,), (0,)), ((), ())), preferred_element_type=jnp.float32
    )


def on_device(
    grid_feats, station_values, station_tile, station_cell, w_embed, w_first, w_second, cotangent
):
    cells = grid_feats[0]
    rows, cols, chans = cells.shape
    values = station_values[0]
    tiles = station_tile[0, :, 0]
    where = station_cell[0]
    n_tiles = lax.axis_size("row") * lax.axis_size("col")
    count = values.shape[0]
    capacity = max(2, 2 * count // n_tiles)
    slots = n_tiles * capacity
    hits = (tiles[:, None] == jnp.arange(n_tiles, dtype=jnp.int32)[None, :]).astype(jnp.int32)
    ranks = jnp.sum(jnp.cumsum(hits, axis=0) * hits, axis=1) - 1
    target = tiles * capacity + ranks
    chooser = (target[None, :] == jnp.arange(slots, dtype=jnp.int32)[:, None]).astype(jnp.bfloat16)
    chosen = jnp.dot(chooser, values, preferred_element_type=jnp.float32).astype(jnp.bfloat16)
    outgoing = jnp.dot(chosen, w_embed, preferred_element_type=jnp.float32)
    id_parts = jnp.zeros((count, chans), jnp.bfloat16)
    id_parts = id_parts.at[:, 0].set((where // 64 * 64).astype(jnp.bfloat16))
    id_parts = id_parts.at[:, 1].set((where % 64).astype(jnp.bfloat16))
    id_sums = jnp.dot(chooser, id_parts, preferred_element_type=jnp.float32)
    slot_ids = (id_sums[:, 0] + id_sums[:, 1]).reshape(n_tiles, capacity)
    id_row = jnp.zeros((n_tiles, 1, chans), jnp.float32).at[:, 0, :capacity].set(slot_ids)
    payload = jnp.concatenate([outgoing.reshape(n_tiles, capacity, chans), id_row], axis=1)
    arrived = lax.all_to_all(payload, ("row", "col"), split_axis=0, concat_axis=0, tiled=True)
    embedded = arrived[:, :capacity, :].reshape(slots, chans)
    arrived_ids = arrived[:, capacity, :capacity].reshape(slots)
    spread = (
        arrived_ids[None, :] == jnp.arange(rows * cols, dtype=jnp.float32)[:, None]
    ).astype(jnp.bfloat16)
    top = lax.reduce_precision(embedded, exponent_bits=8, mantissa_bits=7)
    rest = embedded - top
    middle = lax.reduce_precision(rest, exponent_bits=8, mantissa_bits=7)
    bottom = rest - middle
    split = jnp.concatenate([top, middle, bottom], axis=1).astype(jnp.bfloat16)
    pieces = jnp.dot(spread, split, preferred_element_type=jnp.float32)
    placed = pieces[:, :chans] + pieces[:, chans : 2 * chans] + pieces[:, 2 * chans :]
    first_in = (
        (cells.astype(jnp.float32).reshape(rows * cols, chans) + placed)
        .astype(jnp.bfloat16)
        .reshape(rows, cols, chans)
    )
    w_one = w_first.reshape(9 * chans, chans)
    w_two = w_second.reshape(9 * chans, chans)
    back = cotangent[0]
    padded_back = with_halo(back, (("row", 0), ("col", 1)), 2)
    w_turned = jnp.transpose(w_second[::-1, ::-1], (0, 1, 3, 2)).reshape(9 * chans, chans)
    back_flat = back.reshape(rows * cols, chans)
    grad_act1 = back_flat.astype(jnp.float32) + jnp.dot(
        unfold(padded_back, 2, rows, cols), w_turned, preferred_element_type=jnp.float32
    )
    deep = with_halo(first_in, (("row", 0), ("col", 1)), 3)
    deep, grad_act1 = lax.optimization_barrier((deep, grad_act1))
    pre_wide = jnp.dot(
        unfold(deep, 1, rows + 4, cols + 4), w_one, preferred_element_type=jnp.float32
    ).reshape(rows + 4, cols + 4, chans)
    row_ids = lax.axis_index("row") * rows - 2 + jnp.arange(rows + 4, dtype=jnp.int32)
    col_ids = lax.axis_index("col") * cols - 2 + jnp.arange(cols + 4, dtype=jnp.int32)
    inside_rows = (row_ids >= 0) & (row_ids < rows * lax.axis_size("row"))
    inside_cols = (col_ids >= 0) & (col_ids < cols * lax.axis_size("col"))
    inside = inside_rows[:, None] & inside_cols[None, :]
    padded1 = jnp.where(inside[:, :, None], jax.nn.silu(pre_wide), 0.0).astype(jnp.bfloat16)
    pre1 = pre_wide[2:-2, 2:-2].reshape(rows * cols, chans)
    act1 = padded1[2:-2, 2:-2]
    patches0 = unfold(deep[2:-2, 2:-2], 1, rows, cols)
    patches1 = unfold(padded1, 2, rows, cols)
    sigmoid_pre = jax.nn.sigmoid(pre1)
    grad_pre1 = (grad_act1 * sigmoid_pre * (1.0 + pre1 * (1.0 - sigmoid_pre))).astype(jnp.bfloat16)
    grad_pre1 = lax.optimization_barrier(grad_pre1)
    first_term = contract_rows(patches0, grad_pre1)
    second_term = contract_rows(patches1, back_flat)
    total_cells = (
        rows
        * lax.axis_size("row")
        * cols
        * lax.axis_size("col")
        * lax.axis_size("batch")
        * cells_per_sample_factor(grid_feats)
    )
    scale = 1.0 / math.sqrt(total_cells)
    terms = jnp.concatenate([first_term, second_term]) * scale
    pre2 = jnp.dot(patches1, w_two, preferred_element_type=jnp.float32)
    output = (
        (act1.astype(jnp.float32).reshape(rows * cols, chans) + pre2)
        .astype(jnp.bfloat16)
        .reshape(1, rows, cols, chans)
    )
    summed, output = tree_sum(terms, output)
    first_sum, second_sum = jnp.split(summed, 2)
    grad_first = first_sum.reshape(3, 3, chans, chans)
    grad_second = second_sum.reshape(3, 3, chans, chans)
    return (output, grad_first, grad_second)


def cells_per_sample_factor(grid_feats):
    return grid_feats.shape[0]


def solution(mesh):
    return jax.shard_map(
        on_device,
        mesh=mesh,
        in_specs=(
            P("batch", "row", "col", None),
            P("batch", ("row", "col"), None),
            P("batch", ("row", "col"), None),
            P("batch", ("row", "col")),
            P(),
            P(),
            P(),
            P("batch", "row", "col", None),
        ),
        out_specs=(P("batch", "row", "col", None), P(), P()),
        check_vma=False,
    )
```
